256 devices in a mesh: leaf: 256 (over y, x, z, core).
Axes of the slice: x: 4, y: 4, z: 8, core: 2. Of those that a mesh axis runs over, the one named last changes fastest.
Arguments:
- vectors: bfloat16 [1048576, 64], P('leaf'), may hold values from -6 to 6
- contexts: float32 [8, 1048576], P(None, 'leaf'), may hold values from -6 to 6
- tree_order: int32 [256, 4096], P('leaf'), may hold values from 0 to 4095, each once within a row
- live_counts: int32 [512], P('leaf'), may hold values from 1024 to 2048, as said below
- level_bases: bfloat16 [9, 1048576, 128], P(None, 'leaf'), may hold values from -6 to 6
- coupling: float32 [9, 128], replicated, may hold values from 0.3 to 1.5
- length_scale: float32 [8], replicated, may hold values from 0.7 to 2
Outputs:
- kernel_product: bfloat16 [1048576, 64], P('leaf')
The draws below stay inside these ranges and needn't reach their ends.
Inputs may be any that keep to these rules, and one draw needn't show every extreme that they name: `tree_order`: each device's row is a permutation of its 4096 context indices. `live_counts`: some leaf has exactly 1024 live slots and some leaf is full.
All inputs are finite; a program needn't handle non-finite values.
Results may differ from the reference program's by a relative error of at most 0.0048.
Values sent between devices are 32-bit elements; how exact they have to be, the bound alone decides.
No kernel may reach another device: no remote copies, remote signals or barrier semaphores. Data moves between devices by JAX's collectives and lax.ppermute only.
A program may use at most 64 MiB of HBM per device.

```python
import math
import jax
import jax.numpy as jnp
from jax import lax

LEAF = 2048
RANK = 128
PANEL = 64
DIM = 8
PTS_DEV = 4096
LEVELS = 9
LEAVES = 512
POINTS = 1048576
N_LEAF = 256


def draw_live_counts(key, part):
    first_key = jax.random.fold_in(key, 11)
    second_key = jax.random.fold_in(key, 12)
    counts = LEAF - jax.random.randint(first_key, (LEAVES,), 0, LEAF // 2 + 1)
    picked = jax.random.permutation(second_key, LEAVES)
    counts = counts.at[picked[0]].set(LEAF)
    counts = counts.at[picked[1]].set(LEAF // 2)
    return counts.astype(jnp.int32)


def steps_of(own_key, shape, cuts, least, high):
    def one(position, parts):
        heights = jax.random.uniform(jax.random.fold_in(jax.random.fold_in(own_key, 6), position), (parts,), jnp.float32, least / len(cuts), high / len(cuts))
        return jnp.repeat(jnp.exp(heights), shape[position] // parts).reshape((-1,) + (1,) * (len(shape) - position - 1))

    level = one(*cuts[0])
    for cut in cuts[1:]:
        level = level * one(*cut)
    return level


def centred(rng, dims, scale, bound, cuts=(), kind=jnp.bfloat16):
    gain = steps_of(rng, dims, cuts, -0.22, 0.18) if cuts else 1.0
    array = jax.random.normal(rng, dims, jnp.float32) * scale * gain
    return jnp.minimum(jnp.maximum(array, -bound), bound).astype(kind)


def setup_inputs(seed: int = 0) -> dict:
    streams_of = jax.random.split(jax.random.key(seed), 8)
    return {
        "vectors": centred(streams_of[0], (POINTS, PANEL), 1.0, 6.0, ((0, 256),)),
        "contexts": centred(streams_of[1], (DIM, POINTS), 1.0, 6.0, ((1, 256),), jnp.float32),
        "tree_order": jax.vmap(lambda own: jax.random.permutation(own, PTS_DEV))(jax.random.split(streams_of[2], N_LEAF)).reshape((N_LEAF, PTS_DEV)).astype(jnp.int32),
        "live_counts": draw_live_counts(jax.random.fold_in(streams_of[7], 71), 0),
        "level_bases": centred(streams_of[4], (LEVELS, POINTS, RANK), 1.0, 6.0, ((1, 256),)),
        "coupling": jnp.clip(jnp.exp(jax.random.uniform(streams_of[5], (LEVELS, RANK), jnp.float32, math.log(0.3), math.log(1.5))), 0.3, 1.5),
        "length_scale": jnp.clip(jnp.exp(jax.random.uniform(streams_of[6], (DIM,), jnp.float32, math.log(0.7), math.log(2.0))), 0.7, 2.0),
    }


root_three = math.sqrt(3.0)

def matern_block(row_points, col_points):
    squared = jnp.zeros((row_points.shape[1], col_points.shape[1]), jnp.float32)
    for coord_index in range(row_points.shape[0]):
        offset = row_points[coord_index][:, None] - col_points[coord_index][None, :]
        squared = squared + offset * offset
    scaled = root_three * jnp.sqrt(squared)
    return ((1.0 + scaled) * jnp.exp(-scaled)).astype(jnp.bfloat16)

def reference(vectors, contexts, tree_order, live_counts, level_bases, coupling, length_scale):
    points = vectors.shape[0]
    per_device = tree_order.shape[1]
    offsets = (jnp.arange(tree_order.shape[0], dtype=jnp.int32) * per_device)[:, None]
    global_order = (tree_order + offsets).reshape(-1).astype(jnp.int32)
    ordered = jnp.take(vectors, global_order, axis=0)
    scaled_points = jnp.take(contexts, global_order, axis=1) / length_scale[:, None]
    slot_limit = jnp.repeat(live_counts, LEAF)
    within = jnp.arange(points, dtype=jnp.int32) % LEAF
    live_rows = (within < slot_limit)[:, None]
    masked = jnp.where(live_rows, ordered, jnp.zeros_like(ordered))
    leaves = points // LEAF
    leaf_points = scaled_points.reshape(DIM, leaves, LEAF).transpose(1, 0, 2)
    leaf_vectors = masked.reshape(leaves, LEAF, PANEL)

    def dense_leaf(members):
        return jnp.dot(matern_block(members[0], members[0]), members[1], preferred_element_type=jnp.float32)
    accumulated = lax.map(dense_leaf, (leaf_points, leaf_vectors)).reshape(points, PANEL)

    def project(members):
        return lax.dot_general(members[1], members[0], (((0,), (0,)), ((), ())), preferred_element_type=jnp.float32)

    def expand(members):
        return lax.dot_general(members[0], members[1], (((1,), (1,)), ((), ())), preferred_element_type=jnp.float32)
    for level_index in range(LEVELS):
        node_rows = LEAF * 2 ** level_index
        node_count = points // node_rows
        basis_nodes = level_bases[level_index].reshape(node_count, node_rows, RANK)
        vector_nodes = masked.reshape(node_count, node_rows, PANEL)
        node_sums = lax.map(project, (basis_nodes, vector_nodes))
        node_coef = node_sums * (1.0 / math.sqrt(node_rows))
        sibling = node_coef.reshape(node_count // 2, 2, PANEL, RANK)[:, ::-1].reshape(node_count, PANEL, RANK)
        weights = (sibling * (coupling[level_index] / math.sqrt(RANK))).astype(jnp.bfloat16)
        accumulated = accumulated + lax.map(expand, (basis_nodes, weights)).reshape(points, PANEL)
    result = jnp.where(live_rows, accumulated, jnp.zeros_like(accumulated)).astype(jnp.bfloat16)
    inverse = jnp.zeros((points,), jnp.int32).at[global_order].set(jnp.arange(points, dtype=jnp.int32))
    return jnp.take(result, inverse, axis=0)
```

```python
import math

import jax
import jax.numpy as jnp
from jax import lax
from jax.sharding import PartitionSpec as P

LEAF = 2048
RANK = 128
PANEL = 64
DIM = 8


root_three = math.sqrt(3.0)


def swapped(x, axis, bit):
    return lax.ppermute(x, axis, [(i, i ^ 1 << bit) for i in range(lax.axis_size(axis))])


def matern_block(row_points, col_points):
    squared = jnp.zeros((row_points.shape[1], col_points.shape[1]), jnp.float32)
    for coord_index in range(row_points.shape[0]):
        offset = row_points[coord_index][:, None] - col_points[coord_index][None, :]
        squared = squared + offset * offset
    scaled = root_three * jnp.sqrt(squared)
    return ((1.0 + scaled) * jnp.exp(-scaled)).astype(jnp.bfloat16)


def body(vectors, contexts, tree_order, live_counts, level_bases, coupling, length_scale):
    per_device = vectors.shape[0]
    leaf_count = live_counts.shape[0]
    local_levels = leaf_count.bit_length() - 1
    device_levels = lax.axis_size("leaf").bit_length() - 1
    slot_order = tree_order[0]
    ordered = jnp.take(vectors, slot_order, axis=0)
    scaled_points = jnp.take(contexts, slot_order, axis=1) / length_scale[:, None]
    slot_limit = jnp.repeat(live_counts, LEAF)
    within = jnp.arange(per_device, dtype=jnp.int32) % LEAF
    live_rows = (within < slot_limit)[:, None]
    masked = jnp.where(live_rows, ordered, jnp.zeros_like(ordered))

    partials = jnp.einsum(
        "rp,lrk->lpk", masked, level_bases[local_levels:], preferred_element_type=jnp.float32
    )
    block_rows = min(512, LEAF)
    chunks = []
    for leaf_index in range(leaf_count):
        for block_start in range(0, LEAF, block_rows):
            chunks.append((leaf_index, block_start))

    def dense_chunk(points, vectors_here, block_start):
        kernel = matern_block(points[:, block_start : block_start + block_rows], points)
        return jnp.dot(kernel, vectors_here, preferred_element_type=jnp.float32)

    stack = partials
    finished = []
    pieces = [None] * len(chunks)
    gate = None
    for bit_index in range(device_levels):
        received = swapped(stack, "leaf", bit_index)
        for chunk_index in range(len(chunks)):
            if chunk_index * device_levels // len(chunks) != bit_index or pieces[chunk_index] is not None:
                continue
            leaf_index, block_start = chunks[chunk_index]
            points = scaled_points[:, leaf_index * LEAF : (leaf_index + 1) * LEAF]
            vectors_here = masked[leaf_index * LEAF : (leaf_index + 1) * LEAF]
            if gate is not None:
                gate, points, vectors_here = lax.optimization_barrier((gate, points, vectors_here))
            pieces[chunk_index] = dense_chunk(points, vectors_here, block_start)
        finished.append(received[0])
        stack = stack[1:] + received[1:]
        gate = received
    for chunk_index in range(len(chunks)):
        if pieces[chunk_index] is None:
            leaf_index, block_start = chunks[chunk_index]
            points = scaled_points[:, leaf_index * LEAF : (leaf_index + 1) * LEAF]
            vectors_here = masked[leaf_index * LEAF : (leaf_index + 1) * LEAF]
            pieces[chunk_index] = dense_chunk(points, vectors_here, block_start)
    sibling_totals = jnp.stack(finished)
    accumulated = jnp.concatenate(pieces, axis=0)

    level_index = 0
    node_rows = LEAF * 2**level_index
    node_count = per_device // node_rows
    basis_nodes = level_bases[level_index].reshape(node_count, node_rows, RANK)
    vector_nodes = masked.reshape(node_count, node_rows, PANEL)
    node_sums = jnp.einsum(
        "nrp,nrk->npk", vector_nodes, basis_nodes, preferred_element_type=jnp.float32
    )
    node_coef = node_sums * (1.0 / math.sqrt(node_rows))
    sibling = node_coef.reshape(node_count // 2, 2, PANEL, RANK)[:, ::-1].reshape(
        node_count, PANEL, RANK
    )
    weights = (sibling * (coupling[level_index] / math.sqrt(RANK))).astype(jnp.bfloat16)
    accumulated = accumulated + jnp.einsum(
        "nrk,npk->nrp", basis_nodes, weights, preferred_element_type=jnp.float32
    ).reshape(per_device, PANEL)

    node_scale = jnp.array(
        [1.0 / math.sqrt(LEAF * 2 ** (local_levels + s)) for s in range(device_levels)],
        jnp.float32,
    )[:, None, None]
    node_coef = sibling_totals * node_scale
    weights = (node_coef * (coupling[local_levels:, None, :] / math.sqrt(RANK))).astype(
        jnp.bfloat16
    )
    accumulated = accumulated + jnp.einsum(
        "lrk,lpk->rp", level_bases[local_levels:], weights, preferred_element_type=jnp.float32
    )
    result = jnp.where(live_rows, accumulated, jnp.zeros_like(accumulated)).astype(jnp.bfloat16)
    inverse = (
        jnp.zeros((per_device,), jnp.int32)
        .at[slot_order]
        .set(jnp.arange(per_device, dtype=jnp.int32))
    )
    return jnp.take(result, inverse, axis=0)


def solution(mesh):
    in_specs = (
        P("leaf", None),
        P(None, "leaf"),
        P("leaf", None),
        P("leaf"),
        P(None, "leaf", None),
        P(),
        P(),
    )
    out_specs = P("leaf", None)
    return jax.shard_map(body, mesh=mesh, in_specs=in_specs, out_specs=out_specs, check_vma=False)
```

```python
import math

import jax
import jax.numpy as jnp
from jax import lax
from jax.experimental import pallas as pl
from jax.sharding import PartitionSpec as P

LEAF = 2048
RANK = 128
PANEL = 64
DIM = 8


root_three = math.sqrt(3.0)
FEATURES = 64
BLOCK = 256
BUTTERFLY_LEVELS = 4


def gram_features(points):
    def split(value):
        high = lax.reduce_precision(value, exponent_bits=8, mantissa_bits=7)
        rest = value - high
        middle = lax.reduce_precision(rest, exponent_bits=8, mantissa_bits=7)
        low = rest - middle
        return (
            high.astype(jnp.bfloat16),
            middle.astype(jnp.bfloat16),
            low.astype(jnp.bfloat16),
        )

    norm = jnp.zeros_like(points[0])
    for coord_index in range(points.shape[0]):
        norm = norm + points[coord_index] * points[coord_index]
    high, middle, low = split(points)
    norm_parts = jnp.stack(split(norm))
    ones = jnp.ones((3, points.shape[1]), jnp.bfloat16)
    pad = jnp.zeros((FEATURES - 6 * DIM - 6, points.shape[1]), jnp.bfloat16)
    twice = lambda part: part * jnp.asarray(-2.0, jnp.bfloat16)
    lhs = jnp.concatenate(
        [twice(high), twice(high), twice(middle), twice(middle), twice(high), twice(low), norm_parts, ones, pad]
    )
    rhs = jnp.concatenate([high, middle, high, middle, low, high, ones, norm_parts, pad])
    return lhs.T, rhs


def dense_kernel(lhs_ref, rhs_ref, vec_ref, out_ref):
    squared = jnp.dot(lhs_ref[...], rhs_ref[...], preferred_element_type=jnp.float32)
    scaled = root_three * jnp.sqrt(jnp.maximum(squared, 0.0))
    kernel = ((1.0 + scaled) * jnp.exp(-scaled)).astype(jnp.bfloat16)
    out_ref[...] = jnp.dot(kernel, vec_ref[...], preferred_element_type=jnp.float32)


def dense_rows(lhs, rhs, vec, row_start, rows):
    leaf = row_start // LEAF
    first = row_start // BLOCK
    return pl.pallas_call(
        dense_kernel,
        grid=(rows // BLOCK,),
        in_specs=[
            pl.BlockSpec((BLOCK, FEATURES), lambda i: (first + i, 0)),
            pl.BlockSpec((FEATURES, LEAF), lambda i: (0, leaf)),
            pl.BlockSpec((LEAF, PANEL), lambda i: (leaf, 0)),
        ],
        out_specs=pl.BlockSpec((BLOCK, PANEL), lambda i: (i, 0)),
        out_shape=jax.ShapeDtypeStruct((rows, PANEL), jnp.float32),
    )(lhs, rhs, vec)


def swapped(x, axis, bit):
    return lax.ppermute(x, axis, [(i, i ^ 1 << bit) for i in range(lax.axis_size(axis))])


def gram_features(points):
    def split(value):
        high = lax.reduce_precision(value, exponent_bits=8, mantissa_bits=7)
        rest = value - high
        middle = lax.reduce_precision(rest, exponent_bits=8, mantissa_bits=7)
        low = rest - middle
        return (
            high.astype(jnp.bfloat16),
            middle.astype(jnp.bfloat16),
            low.astype(jnp.bfloat16),
        )

    norm = jnp.zeros_like(points[0])
    for coord_index in range(points.shape[0]):
        norm = norm + points[coord_index] * points[coord_index]
    high, middle, low = split(points)
    norm_parts = jnp.stack(split(norm))
    ones = jnp.ones((3, points.shape[1]), jnp.bfloat16)
    pad = jnp.zeros((FEATURES - 6 * DIM - 6, points.shape[1]), jnp.bfloat16)
    twice = lambda part: part * jnp.asarray(-2.0, jnp.bfloat16)
    lhs = jnp.concatenate(
        [twice(high), twice(high), twice(middle), twice(middle), twice(high), twice(low), norm_parts, ones, pad]
    )
    rhs = jnp.concatenate([high, middle, high, middle, low, high, ones, norm_parts, pad])
    return lhs, rhs


def dense_kernel(lhs_ref, rhs_ref, vec_ref, out_ref):
    squared = jnp.dot(lhs_ref[...], rhs_ref[...], preferred_element_type=jnp.float32)
    scaled = root_three * jnp.sqrt(jnp.maximum(squared, 0.0))
    kernel = ((1.0 + scaled) * jnp.exp(-scaled)).astype(jnp.bfloat16)
    out_ref[...] = jnp.dot(kernel, vec_ref[...], preferred_element_type=jnp.float32)


def dense_leaves(lhs, rhs, vec):
    rows = lhs.shape[0]
    per_leaf = LEAF // BLOCK
    return pl.pallas_call(
        dense_kernel,
        grid=(rows // BLOCK,),
        in_specs=[
            pl.BlockSpec((BLOCK, FEATURES), lambda i: (i, 0)),
            pl.BlockSpec((FEATURES, LEAF), lambda i: (0, i // per_leaf)),
            pl.BlockSpec((LEAF, PANEL), lambda i: (i // per_leaf, 0)),
        ],
        out_specs=pl.BlockSpec((BLOCK, PANEL), lambda i: (i, 0)),
        out_shape=jax.ShapeDtypeStruct((rows, PANEL), jnp.float32),
    )(lhs, rhs, vec)


def body(vectors, contexts, tree_order, live_counts, level_bases, coupling, length_scale):
    per_device = vectors.shape[0]
    leaf_count = live_counts.shape[0]
    local_levels = leaf_count.bit_length() - 1
    device_count = lax.axis_size("leaf")
    device_levels = device_count.bit_length() - 1
    slot_order = tree_order[0]
    onehot = (slot_order[:, None] == jnp.arange(per_device, dtype=jnp.int32)[None, :]).astype(
        jnp.bfloat16
    )
    lhs_features, rhs_features = gram_features(contexts / length_scale[:, None])
    gathered = lax.dot_general(
        onehot,
        jnp.concatenate([vectors, lhs_features.T], axis=1),
        (((1,), (0,)), ((), ())),
        preferred_element_type=jnp.float32,
    ).astype(jnp.bfloat16)
    ordered = gathered[:, :PANEL]
    lhs = gathered[:, PANEL:]
    rhs = lax.dot_general(
        rhs_features, onehot, (((1,), (1,)), ((), ())), preferred_element_type=jnp.float32
    ).astype(jnp.bfloat16)
    slot_limit = jnp.repeat(live_counts, LEAF)
    within = jnp.arange(per_device, dtype=jnp.int32) % LEAF
    live_rows = (within < slot_limit)[:, None]
    masked = jnp.where(live_rows, ordered, jnp.zeros_like(ordered))

    partials = jnp.einsum(
        "rp,lrk->lpk", masked, level_bases[local_levels:], preferred_element_type=jnp.float32
    )
    split_level = min(BUTTERFLY_LEVELS, device_levels)
    stack = partials[:split_level]
    finished = []
    for bit_index in range(split_level):
        received = swapped(stack, "leaf", bit_index)
        finished.append(received[0])
        stack = stack[1:] + received[1:]
    me = lax.axis_index("leaf")
    slots = []
    for step_index in range(split_level, device_levels):
        count = device_count >> step_index
        hot = (jnp.arange(count, dtype=jnp.int32) == (me >> step_index)).astype(jnp.float32)
        slots.append(hot[:, None, None] * partials[step_index][None])
    if slots:
        summed = lax.psum(jnp.concatenate(slots), "leaf")
        offset = 0
        for step_index in range(split_level, device_levels):
            count = device_count >> step_index
            finished.append(
                lax.dynamic_index_in_dim(summed, offset + ((me >> step_index) ^ 1), 0, keepdims=False)
            )
            offset += count
    sibling_totals = jnp.stack(finished)

    accumulated = dense_leaves(lhs, rhs, masked)

    level_index = 0
    node_rows = LEAF * 2**level_index
    node_count = per_device // node_rows
    basis_nodes = level_bases[level_index].reshape(node_count, node_rows, RANK)
    vector_nodes = masked.reshape(node_count, node_rows, PANEL)
    node_sums = jnp.einsum(
        "nrp,nrk->npk", vector_nodes, basis_nodes, preferred_element_type=jnp.float32
    )
    node_coef = node_sums * (1.0 / math.sqrt(node_rows))
    sibling = node_coef.reshape(node_count // 2, 2, PANEL, RANK)[:, ::-1].reshape(
        node_count, PANEL, RANK
    )
    weights = (sibling * (coupling[level_index] / math.sqrt(RANK))).astype(jnp.bfloat16)
    accumulated = accumulated + jnp.einsum(
        "nrk,npk->nrp", basis_nodes, weights, preferred_element_type=jnp.float32
    ).reshape(per_device, PANEL)

    node_scale = jnp.array(
        [1.0 / math.sqrt(LEAF * 2 ** (local_levels + s)) for s in range(device_levels)],
        jnp.float32,
    )[:, None, None]
    node_coef = sibling_totals * node_scale
    weights = (node_coef * (coupling[local_levels:, None, :] / math.sqrt(RANK))).astype(
        jnp.bfloat16
    )
    accumulated = accumulated + jnp.einsum(
        "lrk,lpk->rp", level_bases[local_levels:], weights, preferred_element_type=jnp.float32
    )
    result = jnp.where(live_rows, accumulated, jnp.zeros_like(accumulated)).astype(jnp.bfloat16)
    return lax.dot_general(
        onehot, result, (((0,), (0,)), ((), ())), preferred_element_type=jnp.float32
    ).astype(jnp.bfloat16)


def solution(mesh):
    in_specs = (
        P("leaf", None),
        P(None, "leaf"),
        P("leaf", None),
        P("leaf"),
        P(None, "leaf", None),
        P(),
        P(),
    )
    out_specs = P("leaf", None)
    return jax.shard_map(body, mesh=mesh, in_specs=in_specs, out_specs=out_specs, check_vma=False)
```

```python
import math

import jax
import jax.numpy as jnp
from jax import lax
from jax.experimental import pallas as pl
from jax.sharding import PartitionSpec as P

LEAF = 2048
RANK = 128
PANEL = 64
DIM = 8


root_three = math.sqrt(3.0)
FEATURES = 64
BLOCK = 256


def swapped(x, axis, bit):
    return lax.ppermute(x, axis, [(i, i ^ 1 << bit) for i in range(lax.axis_size(axis))])


def gram_features(points):
    def split(value):
        high = lax.reduce_precision(value, exponent_bits=8, mantissa_bits=7)
        rest = value - high
        middle = lax.reduce_precision(rest, exponent_bits=8, mantissa_bits=7)
        low = rest - middle
        return (
            high.astype(jnp.bfloat16),
            middle.astype(jnp.bfloat16),
            low.astype(jnp.bfloat16),
        )

    norm = jnp.zeros_like(points[0])
    for coord_index in range(points.shape[0]):
        norm = norm + points[coord_index] * points[coord_index]
    high, middle, low = split(points)
    norm_parts = jnp.stack(split(norm))
    ones = jnp.ones((3, points.shape[1]), jnp.bfloat16)
    pad = jnp.zeros((FEATURES - 6 * DIM - 6, points.shape[1]), jnp.bfloat16)
    twice = lambda part: part * jnp.asarray(-2.0, jnp.bfloat16)
    lhs = jnp.concatenate(
        [twice(high), twice(high), twice(middle), twice(middle), twice(high), twice(low), norm_parts, ones, pad]
    )
    rhs = jnp.concatenate([high, middle, high, middle, low, high, ones, norm_parts, pad])
    return lhs.T, rhs


def dense_kernel(lhs_ref, rhs_ref, vec_ref, gate_ref, acc_ref, out_ref):
    del gate_ref, acc_ref
    squared = jnp.dot(lhs_ref[...], rhs_ref[...], preferred_element_type=jnp.float32)
    scaled = root_three * jnp.sqrt(jnp.maximum(squared, 0.0))
    kernel = ((1.0 + scaled) * jnp.exp(-scaled)).astype(jnp.bfloat16)
    out_ref[...] = jnp.dot(kernel, vec_ref[...], preferred_element_type=jnp.float32)


def dense_rows(acc, lhs, rhs, vec, gate, row_start, rows):
    leaf = row_start // LEAF
    first = row_start // BLOCK
    return pl.pallas_call(
        dense_kernel,
        grid=(rows // BLOCK,),
        in_specs=[
            pl.BlockSpec((BLOCK, FEATURES), lambda i: (first + i, 0)),
            pl.BlockSpec((FEATURES, LEAF), lambda i: (0, leaf)),
            pl.BlockSpec((LEAF, PANEL), lambda i: (leaf, 0)),
            pl.BlockSpec(memory_space=pl.ANY),
            pl.BlockSpec(memory_space=pl.ANY),
        ],
        out_specs=pl.BlockSpec((BLOCK, PANEL), lambda i: (first + i, 0)),
        out_shape=jax.ShapeDtypeStruct(acc.shape, jnp.float32),
        input_output_aliases={4: 0},
    )(lhs, rhs, vec, gate, acc)


def body(vectors, contexts, tree_order, live_counts, level_bases, coupling, length_scale):
    per_device = vectors.shape[0]
    leaf_count = live_counts.shape[0]
    local_levels = leaf_count.bit_length() - 1
    device_count = lax.axis_size("leaf")
    device_levels = device_count.bit_length() - 1
    slot_order = tree_order[0]
    onehot = (slot_order[:, None] == jnp.arange(per_device, dtype=jnp.int32)[None, :]).astype(
        jnp.bfloat16
    )
    lhs_features, _ = gram_features(contexts / length_scale[:, None])
    gathered = lax.dot_general(
        onehot,
        jnp.concatenate([vectors, lhs_features], axis=1),
        (((1,), (0,)), ((), ())),
        preferred_element_type=jnp.float32,
    ).astype(jnp.bfloat16)
    ordered = gathered[:, :PANEL]
    lhs = gathered[:, PANEL:]
    half = jnp.asarray(-0.5, jnp.bfloat16)
    high = lhs[:, 0:DIM] * half
    middle = lhs[:, 2 * DIM : 3 * DIM] * half
    low = lhs[:, 5 * DIM : 6 * DIM] * half
    norm_parts = lhs[:, 6 * DIM : 6 * DIM + 3]
    ones = lhs[:, 6 * DIM + 3 : 6 * DIM + 6]
    rhs = jnp.concatenate(
        [high, middle, high, middle, low, high, ones, norm_parts, lhs[:, 6 * DIM + 6 :]], axis=1
    ).T
    slot_limit = jnp.repeat(live_counts, LEAF)
    within = jnp.arange(per_device, dtype=jnp.int32) % LEAF
    live_rows = (within < slot_limit)[:, None]
    masked = jnp.where(live_rows, ordered, jnp.zeros_like(ordered))

    partials = jnp.einsum(
        "rp,lrk->lpk", masked, level_bases[local_levels:], preferred_element_type=jnp.float32
    )
    block_rows = min(512, LEAF)
    chunk_starts = list(range(0, per_device, block_rows))
    accumulated = jnp.zeros((per_device, PANEL), jnp.float32)
    stack = partials
    finished = []
    gate = jnp.zeros((8, RANK), jnp.float32)
    done = 0
    for bit_index in range(device_levels):
        received = swapped(stack, "leaf", bit_index)
        upto = (bit_index + 1) * len(chunk_starts) // device_levels
        for row_start in chunk_starts[done:upto]:
            accumulated = dense_rows(accumulated, lhs, rhs, masked, gate, row_start, block_rows)
        done = upto
        finished.append(received[0])
        stack = stack[1:] + received[1:]
        gate = received[0, :8]
    for row_start in chunk_starts[done:]:
        accumulated = dense_rows(accumulated, lhs, rhs, masked, gate, row_start, block_rows)
    sibling_totals = jnp.stack(finished)


    level_index = 0
    node_rows = LEAF * 2**level_index
    node_count = per_device // node_rows
    basis_nodes = level_bases[level_index].reshape(node_count, node_rows, RANK)
    vector_nodes = masked.reshape(node_count, node_rows, PANEL)
    node_sums = jnp.einsum(
        "nrp,nrk->npk", vector_nodes, basis_nodes, preferred_element_type=jnp.float32
    )
    node_coef = node_sums * (1.0 / math.sqrt(node_rows))
    sibling = node_coef.reshape(node_count // 2, 2, PANEL, RANK)[:, ::-1].reshape(
        node_count, PANEL, RANK
    )
    weights = (sibling * (coupling[level_index] / math.sqrt(RANK))).astype(jnp.bfloat16)
    accumulated = accumulated + jnp.einsum(
        "nrk,npk->nrp", basis_nodes, weights, preferred_element_type=jnp.float32
    ).reshape(per_device, PANEL)

    node_scale = jnp.array(
        [1.0 / math.sqrt(LEAF * 2 ** (local_levels + s)) for s in range(device_levels)],
        jnp.float32,
    )[:, None, None]
    node_coef = sibling_totals * node_scale
    weights = (node_coef * (coupling[local_levels:, None, :] / math.sqrt(RANK))).astype(
        jnp.bfloat16
    )
    accumulated = accumulated + jnp.einsum(
        "lrk,lpk->rp", level_bases[local_levels:], weights, preferred_element_type=jnp.float32
    )
    result = jnp.where(live_rows, accumulated, jnp.zeros_like(accumulated)).astype(jnp.bfloat16)
    return lax.dot_general(
        onehot, result, (((0,), (0,)), ((), ())), preferred_element_type=jnp.float32
    ).astype(jnp.bfloat16)


def solution(mesh):
    in_specs = (
        P("leaf", None),
        P(None, "leaf"),
        P("leaf", None),
        P("leaf"),
        P(None, "leaf", None),
        P(),
        P(),
    )
    out_specs = P("leaf", None)
    return jax.shard_map(body, mesh=mesh, in_specs=in_specs, out_specs=out_specs, check_vma=False)
```

```python
import math

import jax
import jax.numpy as jnp
from jax import lax
from jax.experimental import pallas as pl
from jax.sharding import PartitionSpec as P

LEAF = 2048
RANK = 128
PANEL = 64
DIM = 8


root_three = math.sqrt(3.0)
FEATURES = 64
BLOCK = 256


def swapped(x, axis, bit):
    return lax.ppermute(x, axis, [(i, i ^ 1 << bit) for i in range(lax.axis_size(axis))])


def gram_features(points):
    def split(value):
        high = lax.reduce_precision(value, exponent_bits=8, mantissa_bits=7)
        rest = value - high
        middle = lax.reduce_precision(rest, exponent_bits=8, mantissa_bits=7)
        low = rest - middle
        return (
            high.astype(jnp.bfloat16),
            middle.astype(jnp.bfloat16),
            low.astype(jnp.bfloat16),
        )

    norm = jnp.zeros_like(points[0])
    for coord_index in range(points.shape[0]):
        norm = norm + points[coord_index] * points[coord_index]
    high, middle, low = split(points)
    norm_parts = jnp.stack(split(norm))
    ones = jnp.ones((3, points.shape[1]), jnp.bfloat16)
    pad = jnp.zeros((FEATURES - 6 * DIM - 6, points.shape[1]), jnp.bfloat16)
    twice = lambda part: part * jnp.asarray(-2.0, jnp.bfloat16)
    lhs = jnp.concatenate(
        [twice(high), twice(high), twice(middle), twice(middle), twice(high), twice(low), norm_parts, ones, pad]
    )
    rhs = jnp.concatenate([high, middle, high, middle, low, high, ones, norm_parts, pad])
    return lhs.T, rhs


def dense_kernel(lhs_ref, rhs_ref, vec_ref, gate_ref, acc_ref, out_ref):
    del gate_ref, acc_ref
    squared = lax.dot_general(
        lhs_ref[...], rhs_ref[...], (((1,), (1,)), ((), ())), preferred_element_type=jnp.float32
    )
    scaled = root_three * jnp.sqrt(jnp.maximum(squared, 0.0))
    kernel = ((1.0 + scaled) * jnp.exp(-scaled)).astype(jnp.bfloat16)
    out_ref[...] = jnp.dot(kernel, vec_ref[...], preferred_element_type=jnp.float32)


def dense_rows(acc, lhs, rhs, vec, gate, row_start, rows):
    leaf = row_start // LEAF
    first = row_start // BLOCK
    return pl.pallas_call(
        dense_kernel,
        grid=(rows // BLOCK,),
        in_specs=[
            pl.BlockSpec((BLOCK, FEATURES), lambda i: (first + i, 0)),
            pl.BlockSpec((LEAF, FEATURES), lambda i: (leaf, 0)),
            pl.BlockSpec((LEAF, PANEL), lambda i: (leaf, 0)),
            pl.BlockSpec(memory_space=pl.ANY),
            pl.BlockSpec(memory_space=pl.ANY),
        ],
        out_specs=pl.BlockSpec((BLOCK, PANEL), lambda i: (first + i, 0)),
        out_shape=jax.ShapeDtypeStruct(acc.shape, jnp.float32),
        input_output_aliases={4: 0},
    )(lhs, rhs, vec, gate, acc)


def body(vectors, contexts, tree_order, live_counts, level_bases, coupling, length_scale):
    per_device = vectors.shape[0]
    leaf_count = live_counts.shape[0]
    local_levels = leaf_count.bit_length() - 1
    device_count = lax.axis_size("leaf")
    device_levels = device_count.bit_length() - 1
    slot_order = tree_order[0]
    onehot = (slot_order[:, None] == jnp.arange(per_device, dtype=jnp.int32)[None, :]).astype(
        jnp.bfloat16
    )
    lhs_features, _ = gram_features(contexts / length_scale[:, None])
    gathered = lax.dot_general(
        onehot,
        jnp.concatenate([vectors, lhs_features], axis=1),
        (((1,), (0,)), ((), ())),
        preferred_element_type=jnp.float32,
    ).astype(jnp.bfloat16)
    ordered = gathered[:, :PANEL]
    lhs = gathered[:, PANEL:]
    half = jnp.asarray(-0.5, jnp.bfloat16)
    high = lhs[:, 0:DIM] * half
    middle = lhs[:, 2 * DIM : 3 * DIM] * half
    low = lhs[:, 5 * DIM : 6 * DIM] * half
    norm_parts = lhs[:, 6 * DIM : 6 * DIM + 3]
    ones = lhs[:, 6 * DIM + 3 : 6 * DIM + 6]
    rhs = jnp.concatenate(
        [high, middle, high, middle, low, high, ones, norm_parts, lhs[:, 6 * DIM + 6 :]], axis=1
    )
    slot_limit = jnp.repeat(live_counts, LEAF)
    within = jnp.arange(per_device, dtype=jnp.int32) % LEAF
    live_rows = (within < slot_limit)[:, None]
    masked = jnp.where(live_rows, ordered, jnp.zeros_like(ordered))

    partials = jnp.einsum(
        "rp,lrk->lpk", masked, level_bases[local_levels:], preferred_element_type=jnp.float32
    )
    block_rows = min(512, LEAF)
    chunk_starts = list(range(0, per_device, block_rows))
    accumulated = jnp.zeros((per_device, PANEL), jnp.float32)
    stack = partials
    finished = []
    gate = jnp.zeros((8, RANK), jnp.float32)
    done = 0
    for bit_index in range(device_levels):
        received = swapped(stack, "leaf", bit_index)
        upto = (bit_index + 1) * len(chunk_starts) // device_levels
        for row_start in chunk_starts[done:upto]:
            accumulated = dense_rows(accumulated, lhs, rhs, masked, gate, row_start, block_rows)
        done = upto
        finished.append(received[0])
        stack = stack[1:] + received[1:]
        gate = received[0, :8]
    for row_start in chunk_starts[done:]:
        accumulated = dense_rows(accumulated, lhs, rhs, masked, gate, row_start, block_rows)
    sibling_totals = jnp.stack(finished)


    level_index = 0
    node_rows = LEAF * 2**level_index
    node_count = per_device // node_rows
    basis_nodes = level_bases[level_index].reshape(node_count, node_rows, RANK)
    vector_nodes = masked.reshape(node_count, node_rows, PANEL)
    node_sums = jnp.einsum(
        "nrp,nrk->npk", vector_nodes, basis_nodes, preferred_element_type=jnp.float32
    )
    node_coef = node_sums * (1.0 / math.sqrt(node_rows))
    sibling = node_coef.reshape(node_count // 2, 2, PANEL, RANK)[:, ::-1].reshape(
        node_count, PANEL, RANK
    )
    weights = (sibling * (coupling[level_index] / math.sqrt(RANK))).astype(jnp.bfloat16)
    accumulated = accumulated + jnp.einsum(
        "nrk,npk->nrp", basis_nodes, weights, preferred_element_type=jnp.float32
    ).reshape(per_device, PANEL)

    node_scale = jnp.array(
        [1.0 / math.sqrt(LEAF * 2 ** (local_levels + s)) for s in range(device_levels)],
        jnp.float32,
    )[:, None, None]
    node_coef = sibling_totals * node_scale
    weights = (node_coef * (coupling[local_levels:, None, :] / math.sqrt(RANK))).astype(
        jnp.bfloat16
    )
    accumulated = accumulated + jnp.einsum(
        "lrk,lpk->rp", level_bases[local_levels:], weights, preferred_element_type=jnp.float32
    )
    result = jnp.where(live_rows, accumulated, jnp.zeros_like(accumulated)).astype(jnp.bfloat16)
    return lax.dot_general(
        onehot, result, (((0,), (0,)), ((), ())), preferred_element_type=jnp.float32
    ).astype(jnp.bfloat16)


def solution(mesh):
    in_specs = (
        P("leaf", None),
        P(None, "leaf"),
        P("leaf", None),
        P("leaf"),
        P(None, "leaf", None),
        P(),
        P(),
    )
    out_specs = P("leaf", None)
    return jax.shard_map(body, mesh=mesh, in_specs=in_specs, out_specs=out_specs, check_vma=False)
```

```python
import math

import jax
import jax.numpy as jnp
from jax import lax
from jax.experimental import pallas as pl
from jax.sharding import PartitionSpec as P

LEAF = 2048
RANK = 128
PANEL = 64
DIM = 8


root_three = math.sqrt(3.0)
FEATURES = 64
BLOCK = 256


def swapped(x, axis, bit):
    return lax.ppermute(x, axis, [(i, i ^ 1 << bit) for i in range(lax.axis_size(axis))])


def gram_features(points):
    def split(value):
        high = lax.reduce_precision(value, exponent_bits=8, mantissa_bits=7)
        rest = value - high
        middle = lax.reduce_precision(rest, exponent_bits=8, mantissa_bits=7)
        low = rest - middle
        return (
            high.astype(jnp.bfloat16),
            middle.astype(jnp.bfloat16),
            low.astype(jnp.bfloat16),
        )

    norm = jnp.zeros_like(points[0])
    for coord_index in range(points.shape[0]):
        norm = norm + points[coord_index] * points[coord_index]
    high, middle, low = split(points)
    norm_parts = jnp.stack(split(norm))
    ones = jnp.ones((3, points.shape[1]), jnp.bfloat16)
    pad = jnp.zeros((FEATURES - 6 * DIM - 6, points.shape[1]), jnp.bfloat16)
    twice = lambda part: part * jnp.asarray(-2.0, jnp.bfloat16)
    lhs = jnp.concatenate(
        [twice(high), twice(high), twice(middle), twice(middle), twice(high), twice(low), norm_parts, ones, pad]
    )
    rhs = jnp.concatenate([high, middle, high, middle, low, high, ones, norm_parts, pad])
    return lhs.T, rhs


def dense_kernel(rows_ref, leaf_ref, vec_ref, gate_ref, acc_ref, out_ref):
    del gate_ref, acc_ref
    squared = lax.dot_general(
        rows_ref[:, :FEATURES],
        leaf_ref[:, FEATURES : 2 * FEATURES],
        (((1,), (1,)), ((), ())),
        preferred_element_type=jnp.float32,
    )
    scaled = root_three * jnp.sqrt(jnp.maximum(squared, 0.0))
    kernel = ((1.0 + scaled) * jnp.exp(-scaled)).astype(jnp.bfloat16)
    out_ref[...] = jnp.dot(kernel, vec_ref[...], preferred_element_type=jnp.float32)


def dense_rows(acc, table, vec, gate, row_start, rows):
    leaf = row_start // LEAF
    first = row_start // BLOCK
    width = table.shape[1]
    return pl.pallas_call(
        dense_kernel,
        grid=(rows // BLOCK,),
        in_specs=[
            pl.BlockSpec((BLOCK, width), lambda i: (first + i, 0)),
            pl.BlockSpec((LEAF, width), lambda i: (leaf, 0)),
            pl.BlockSpec((LEAF, PANEL), lambda i: (leaf, 0)),
            pl.BlockSpec(memory_space=pl.ANY),
            pl.BlockSpec(memory_space=pl.ANY),
        ],
        out_specs=pl.BlockSpec((BLOCK, PANEL), lambda i: (first + i, 0)),
        out_shape=jax.ShapeDtypeStruct(acc.shape, jnp.float32),
        input_output_aliases={4: 0},
    )(table, table, vec, gate, acc)


def body(vectors, contexts, tree_order, live_counts, level_bases, coupling, length_scale):
    per_device = vectors.shape[0]
    leaf_count = live_counts.shape[0]
    local_levels = leaf_count.bit_length() - 1
    device_count = lax.axis_size("leaf")
    device_levels = device_count.bit_length() - 1
    slot_order = tree_order[0]
    onehot = (slot_order[:, None] == jnp.arange(per_device, dtype=jnp.int32)[None, :]).astype(
        jnp.bfloat16
    )
    lhs_features, rhs_features = gram_features(contexts / length_scale[:, None])
    table = lax.dot_general(
        onehot,
        jnp.concatenate([lhs_features, rhs_features.T, vectors], axis=1),
        (((1,), (0,)), ((), ())),
        preferred_element_type=jnp.float32,
    ).astype(jnp.bfloat16)
    ordered = table[:, 2 * FEATURES :]
    slot_limit = jnp.repeat(live_counts, LEAF)
    within = jnp.arange(per_device, dtype=jnp.int32) % LEAF
    live_rows = (within < slot_limit)[:, None]
    masked = jnp.where(live_rows, ordered, jnp.zeros_like(ordered))

    partials = jnp.einsum(
        "rp,lrk->lpk", masked, level_bases[local_levels:], preferred_element_type=jnp.float32
    )
    block_rows = min(512, LEAF)
    chunk_starts = list(range(0, per_device, block_rows))
    accumulated = jnp.zeros((per_device, PANEL), jnp.float32)
    stack = partials
    finished = []
    gate = jnp.zeros((8, RANK), jnp.float32)
    done = 0
    for bit_index in range(device_levels):
        received = swapped(stack, "leaf", bit_index)
        upto = (bit_index + 1) * len(chunk_starts) // device_levels
        for row_start in chunk_starts[done:upto]:
            accumulated = dense_rows(accumulated, table, masked, gate, row_start, block_rows)
        done = upto
        finished.append(received[0])
        stack = stack[1:] + received[1:]
        gate = received[0, :8]
    for row_start in chunk_starts[done:]:
        accumulated = dense_rows(accumulated, table, masked, gate, row_start, block_rows)
    sibling_totals = jnp.stack(finished)


    level_index = 0
    node_rows = LEAF * 2**level_index
    node_count = per_device // node_rows
    basis_nodes = level_bases[level_index].reshape(node_count, node_rows, RANK)
    vector_nodes = masked.reshape(node_count, node_rows, PANEL)
    node_sums = jnp.einsum(
        "nrp,nrk->npk", vector_nodes, basis_nodes, preferred_element_type=jnp.float32
    )
    node_coef = node_sums * (1.0 / math.sqrt(node_rows))
    sibling = node_coef.reshape(node_count // 2, 2, PANEL, RANK)[:, ::-1].reshape(
        node_count, PANEL, RANK
    )
    weights = (sibling * (coupling[level_index] / math.sqrt(RANK))).astype(jnp.bfloat16)
    accumulated = accumulated + jnp.einsum(
        "nrk,npk->nrp", basis_nodes, weights, preferred_element_type=jnp.float32
    ).reshape(per_device, PANEL)

    node_scale = jnp.array(
        [1.0 / math.sqrt(LEAF * 2 ** (local_levels + s)) for s in range(device_levels)],
        jnp.float32,
    )[:, None, None]
    node_coef = sibling_totals * node_scale
    weights = (node_coef * (coupling[local_levels:, None, :] / math.sqrt(RANK))).astype(
        jnp.bfloat16
    )
    accumulated = accumulated + jnp.einsum(
        "lrk,lpk->rp", level_bases[local_levels:], weights, preferred_element_type=jnp.float32
    )
    result = jnp.where(live_rows, accumulated, jnp.zeros_like(accumulated)).astype(jnp.bfloat16)
    return lax.dot_general(
        onehot, result, (((0,), (0,)), ((), ())), preferred_element_type=jnp.float32
    ).astype(jnp.bfloat16)


def solution(mesh):
    in_specs = (
        P("leaf", None),
        P(None, "leaf"),
        P("leaf", None),
        P("leaf"),
        P(None, "leaf", None),
        P(),
        P(),
    )
    out_specs = P("leaf", None)
    return jax.shard_map(body, mesh=mesh, in_specs=in_specs, out_specs=out_specs, check_vma=False)
```

```python
import math

import jax
import jax.numpy as jnp
from jax import lax
from jax.experimental import pallas as pl
from jax.sharding import PartitionSpec as P

LEAF = 2048
RANK = 128
PANEL = 64
DIM = 8


root_three = math.sqrt(3.0)
FEATURES = 64
BLOCK = 256


def swapped(x, axis, bit):
    return lax.ppermute(x, axis, [(i, i ^ 1 << bit) for i in range(lax.axis_size(axis))])


def gram_features(points):
    def split(value):
        high = lax.reduce_precision(value, exponent_bits=8, mantissa_bits=7)
        rest = value - high
        middle = lax.reduce_precision(rest, exponent_bits=8, mantissa_bits=7)
        low = rest - middle
        return (
            high.astype(jnp.bfloat16),
            middle.astype(jnp.bfloat16),
            low.astype(jnp.bfloat16),
        )

    norm = jnp.zeros_like(points[0])
    for coord_index in range(points.shape[0]):
        norm = norm + points[coord_index] * points[coord_index]
    high, middle, low = split(points)
    norm_parts = jnp.stack(split(norm))
    ones = jnp.ones((3, points.shape[1]), jnp.bfloat16)
    pad = jnp.zeros((FEATURES - 6 * DIM - 6, points.shape[1]), jnp.bfloat16)
    twice = lambda part: part * jnp.asarray(-2.0, jnp.bfloat16)
    lhs = jnp.concatenate(
        [twice(high), twice(high), twice(middle), twice(middle), twice(high), twice(low), norm_parts, ones, pad]
    )
    rhs = jnp.concatenate([high, middle, high, middle, low, high, ones, norm_parts, pad])
    return lhs.T, rhs


def dense_kernel(rows_ref, leaf_ref, vec_ref, gate_ref, acc_ref, out_ref):
    del gate_ref, acc_ref
    squared = lax.dot_general(
        rows_ref[:, :FEATURES],
        leaf_ref[:, FEATURES : 2 * FEATURES],
        (((1,), (1,)), ((), ())),
        preferred_element_type=jnp.float32,
    )
    scaled = root_three * jnp.sqrt(jnp.maximum(squared, 0.0))
    kernel = ((1.0 + scaled) * jnp.exp(-scaled)).astype(jnp.bfloat16)
    out_ref[...] = jnp.dot(kernel, vec_ref[...], preferred_element_type=jnp.float32)


def dense_rows(acc, table, vec, gate, row_start, rows):
    per_leaf = LEAF // BLOCK
    first = row_start // BLOCK
    width = table.shape[1]
    return pl.pallas_call(
        dense_kernel,
        grid=(rows // BLOCK,),
        in_specs=[
            pl.BlockSpec((BLOCK, width), lambda i: (first + i, 0)),
            pl.BlockSpec((LEAF, width), lambda i: ((first + i) // per_leaf, 0)),
            pl.BlockSpec((LEAF, PANEL), lambda i: ((first + i) // per_leaf, 0)),
            pl.BlockSpec(memory_space=pl.ANY),
            pl.BlockSpec(memory_space=pl.ANY),
        ],
        out_specs=pl.BlockSpec((BLOCK, PANEL), lambda i: (first + i, 0)),
        out_shape=jax.ShapeDtypeStruct(acc.shape, jnp.float32),
        input_output_aliases={4: 0},
    )(table, table, vec, gate, acc)


def body(vectors, contexts, tree_order, live_counts, level_bases, coupling, length_scale):
    per_device = vectors.shape[0]
    leaf_count = live_counts.shape[0]
    local_levels = leaf_count.bit_length() - 1
    device_count = lax.axis_size("leaf")
    device_levels = device_count.bit_length() - 1
    slot_order = tree_order[0]
    onehot = (slot_order[:, None] == jnp.arange(per_device, dtype=jnp.int32)[None, :]).astype(
        jnp.bfloat16
    )
    lhs_features, rhs_features = gram_features(contexts / length_scale[:, None])
    table = lax.dot_general(
        onehot,
        jnp.concatenate([lhs_features, rhs_features.T, vectors], axis=1),
        (((1,), (0,)), ((), ())),
        preferred_element_type=jnp.float32,
    ).astype(jnp.bfloat16)
    ordered = table[:, 2 * FEATURES :]
    slot_limit = jnp.repeat(live_counts, LEAF)
    within = jnp.arange(per_device, dtype=jnp.int32) % LEAF
    live_rows = (within < slot_limit)[:, None]
    masked = jnp.where(live_rows, ordered, jnp.zeros_like(ordered))

    partials = jnp.einsum(
        "rp,lrk->lpk", masked, level_bases[local_levels:], preferred_element_type=jnp.float32
    )
    block_rows = per_device
    chunk_starts = list(range(0, per_device, block_rows))
    accumulated = jnp.zeros((per_device, PANEL), jnp.float32)
    stack = partials
    finished = []
    gate = jnp.zeros((8, RANK), jnp.float32)
    done = 0
    for bit_index in range(device_levels):
        received = swapped(stack, "leaf", bit_index)
        upto = -(-(bit_index + 1) * len(chunk_starts) // device_levels)
        for row_start in chunk_starts[done:upto]:
            accumulated = dense_rows(accumulated, table, masked, gate, row_start, block_rows)
        done = upto
        finished.append(received[0])
        stack = stack[1:] + received[1:]
        gate = received[0, :8]
    for row_start in chunk_starts[done:]:
        accumulated = dense_rows(accumulated, table, masked, gate, row_start, block_rows)
    sibling_totals = jnp.stack(finished)


    level_index = 0
    node_rows = LEAF * 2**level_index
    node_count = per_device // node_rows
    basis_nodes = level_bases[level_index].reshape(node_count, node_rows, RANK)
    vector_nodes = masked.reshape(node_count, node_rows, PANEL)
    node_sums = jnp.einsum(
        "nrp,nrk->npk", vector_nodes, basis_nodes, preferred_element_type=jnp.float32
    )
    node_coef = node_sums * (1.0 / math.sqrt(node_rows))
    sibling = node_coef.reshape(node_count // 2, 2, PANEL, RANK)[:, ::-1].reshape(
        node_count, PANEL, RANK
    )
    weights = (sibling * (coupling[level_index] / math.sqrt(RANK))).astype(jnp.bfloat16)
    accumulated = accumulated + jnp.einsum(
        "nrk,npk->nrp", basis_nodes, weights, preferred_element_type=jnp.float32
    ).reshape(per_device, PANEL)

    node_scale = jnp.array(
        [1.0 / math.sqrt(LEAF * 2 ** (local_levels + s)) for s in range(device_levels)],
        jnp.float32,
    )[:, None, None]
    node_coef = sibling_totals * node_scale
    weights = (node_coef * (coupling[local_levels:, None, :] / math.sqrt(RANK))).astype(
        jnp.bfloat16
    )
    accumulated = accumulated + jnp.einsum(
        "lrk,lpk->rp", level_bases[local_levels:], weights, preferred_element_type=jnp.float32
    )
    result = jnp.where(live_rows, accumulated, jnp.zeros_like(accumulated)).astype(jnp.bfloat16)
    return lax.dot_general(
        onehot, result, (((0,), (0,)), ((), ())), preferred_element_type=jnp.float32
    ).astype(jnp.bfloat16)


def solution(mesh):
    in_specs = (
        P("leaf", None),
        P(None, "leaf"),
        P("leaf", None),
        P("leaf"),
        P(None, "leaf", None),
        P(),
        P(),
    )
    out_specs = P("leaf", None)
    return jax.shard_map(body, mesh=mesh, in_specs=in_specs, out_specs=out_specs, check_vma=False)
```

```python
import math

import jax
import jax.numpy as jnp
from jax import lax
from jax.experimental import pallas as pl
from jax.sharding import PartitionSpec as P

LEAF = 2048
RANK = 128
PANEL = 64
DIM = 8


root_three = math.sqrt(3.0)
FEATURES = 64
BLOCK = 256


def swapped(x, axis, bit):
    return lax.ppermute(x, axis, [(i, i ^ 1 << bit) for i in range(lax.axis_size(axis))])


def gram_features(points):
    def split(value):
        high = lax.reduce_precision(value, exponent_bits=8, mantissa_bits=7)
        rest = value - high
        middle = lax.reduce_precision(rest, exponent_bits=8, mantissa_bits=7)
        low = rest - middle
        return (
            high.astype(jnp.bfloat16),
            middle.astype(jnp.bfloat16),
            low.astype(jnp.bfloat16),
        )

    norm = jnp.zeros_like(points[0])
    for coord_index in range(points.shape[0]):
        norm = norm + points[coord_index] * points[coord_index]
    high, middle, low = split(points)
    norm_parts = jnp.stack(split(norm))
    ones = jnp.ones((3, points.shape[1]), jnp.bfloat16)
    pad = jnp.zeros((FEATURES - 6 * DIM - 6, points.shape[1]), jnp.bfloat16)
    twice = lambda part: part * jnp.asarray(-2.0, jnp.bfloat16)
    lhs = jnp.concatenate(
        [twice(high), twice(high), twice(middle), twice(middle), twice(high), twice(low), norm_parts, ones, pad]
    )
    rhs = jnp.concatenate([high, middle, high, middle, low, high, ones, norm_parts, pad])
    return lhs.T, rhs


def dense_kernel(rows_ref, leaf_ref, vec_ref, gate_ref, acc_ref, out_ref):
    del gate_ref, acc_ref
    squared = lax.dot_general(
        rows_ref[:, :FEATURES],
        leaf_ref[:, FEATURES : 2 * FEATURES],
        (((1,), (1,)), ((), ())),
        preferred_element_type=jnp.float32,
    )
    scaled = root_three * jnp.sqrt(jnp.maximum(squared, 0.0))
    kernel = ((1.0 + scaled) * jnp.exp(-scaled)).astype(jnp.bfloat16)
    out_ref[...] = jnp.dot(kernel, vec_ref[...], preferred_element_type=jnp.float32)


def dense_rows(acc, table, vec, gate, row_start, rows):
    leaf = row_start // LEAF
    first = row_start // BLOCK
    width = table.shape[1]
    return pl.pallas_call(
        dense_kernel,
        grid=(rows // BLOCK,),
        in_specs=[
            pl.BlockSpec((BLOCK, width), lambda i: (first + i, 0)),
            pl.BlockSpec((LEAF, width), lambda i: (leaf, 0)),
            pl.BlockSpec((LEAF, PANEL), lambda i: (leaf, 0)),
            pl.BlockSpec(memory_space=pl.ANY),
            pl.BlockSpec(memory_space=pl.ANY),
        ],
        out_specs=pl.BlockSpec((BLOCK, PANEL), lambda i: (first + i, 0)),
        out_shape=jax.ShapeDtypeStruct(acc.shape, jnp.float32),
        input_output_aliases={4: 0},
    )(table, table, vec, gate, acc)


def body(vectors, contexts, tree_order, live_counts, level_bases, coupling, length_scale):
    per_device = vectors.shape[0]
    leaf_count = live_counts.shape[0]
    local_levels = leaf_count.bit_length() - 1
    device_count = lax.axis_size("leaf")
    device_levels = device_count.bit_length() - 1
    slot_order = tree_order[0]
    onehot = (slot_order[:, None] == jnp.arange(per_device, dtype=jnp.int32)[None, :]).astype(
        jnp.bfloat16
    )
    lhs_features, rhs_features = gram_features(contexts / length_scale[:, None])
    table = lax.dot_general(
        onehot,
        jnp.concatenate([lhs_features, rhs_features.T, vectors], axis=1),
        (((1,), (0,)), ((), ())),
        preferred_element_type=jnp.float32,
    ).astype(jnp.bfloat16)
    ordered = table[:, 2 * FEATURES :]
    slot_limit = jnp.repeat(live_counts, LEAF)
    within = jnp.arange(per_device, dtype=jnp.int32) % LEAF
    live_rows = (within < slot_limit)[:, None]
    masked = jnp.where(live_rows, ordered, jnp.zeros_like(ordered))

    partials = jnp.einsum(
        "rp,lrk->lpk", masked, level_bases[local_levels:], preferred_element_type=jnp.float32
    )
    block_rows = min(512, LEAF)
    chunk_starts = list(range(0, per_device, block_rows))
    accumulated = jnp.zeros((per_device, PANEL), jnp.float32)
    stack = partials
    finished = []
    gate = jnp.zeros((8, RANK), jnp.float32)
    done = 0
    for bit_index in range(device_levels):
        received = swapped(stack, "leaf", bit_index)
        upto = (bit_index + 1) * len(chunk_starts) // device_levels
        for row_start in chunk_starts[done:upto]:
            accumulated = dense_rows(accumulated, table, masked, gate, row_start, block_rows)
        done = upto
        finished.append(received[0])
        stack = stack[1:] + received[1:]
        gate = received[0, :8]
    for row_start in chunk_starts[done:]:
        accumulated = dense_rows(accumulated, table, masked, gate, row_start, block_rows)
    sibling_totals = jnp.stack(finished)


    level_index = 0
    node_rows = LEAF * 2**level_index
    node_count = per_device // node_rows
    basis_nodes = level_bases[level_index].reshape(node_count, node_rows, RANK)
    vector_nodes = masked.reshape(node_count, node_rows, PANEL)
    node_sums = jnp.einsum(
        "nrp,nrk->npk", vector_nodes, basis_nodes, preferred_element_type=jnp.float32
    )
    node_coef = node_sums * (1.0 / math.sqrt(node_rows))
    sibling = node_coef.reshape(node_count // 2, 2, PANEL, RANK)[:, ::-1].reshape(
        node_count, PANEL, RANK
    )
    weights = (sibling * (coupling[level_index] / math.sqrt(RANK))).astype(jnp.bfloat16)
    accumulated = accumulated + jnp.einsum(
        "nrk,npk->nrp", basis_nodes, weights, preferred_element_type=jnp.float32
    ).reshape(per_device, PANEL)

    node_scale = jnp.array(
        [1.0 / math.sqrt(LEAF * 2 ** (local_levels + s)) for s in range(device_levels)],
        jnp.float32,
    )[:, None, None]
    node_coef = sibling_totals * node_scale
    weights = (node_coef * (coupling[local_levels:, None, :] / math.sqrt(RANK))).astype(
        jnp.bfloat16
    )
    accumulated = accumulated + jnp.einsum(
        "lrk,lpk->rp", level_bases[local_levels:], weights, preferred_element_type=jnp.float32
    )
    result = jnp.where(live_rows, accumulated, jnp.zeros_like(accumulated)).astype(jnp.bfloat16)
    inverse = (jnp.arange(per_device, dtype=jnp.int32)[:, None] == slot_order[None, :]).astype(
        jnp.bfloat16
    )
    return jnp.dot(inverse, result, preferred_element_type=jnp.float32).astype(jnp.bfloat16)


def solution(mesh):
    in_specs = (
        P("leaf", None),
        P(None, "leaf"),
        P("leaf", None),
        P("leaf"),
        P(None, "leaf", None),
        P(),
        P(),
    )
    out_specs = P("leaf", None)
    return jax.shard_map(body, mesh=mesh, in_specs=in_specs, out_specs=out_specs, check_vma=False)
```

```python
import math

import jax
import jax.numpy as jnp
from jax import lax
from jax.experimental import pallas as pl
from jax.sharding import PartitionSpec as P

LEAF = 2048
RANK = 128
PANEL = 64
DIM = 8


root_three = math.sqrt(3.0)
FEATURES = 64
BLOCK = 256


def swapped(x, axis, bit):
    return lax.ppermute(x, axis, [(i, i ^ 1 << bit) for i in range(lax.axis_size(axis))])


def gram_features(points):
    def split(value):
        high = lax.reduce_precision(value, exponent_bits=8, mantissa_bits=7)
        rest = value - high
        middle = lax.reduce_precision(rest, exponent_bits=8, mantissa_bits=7)
        low = rest - middle
        return (
            high.astype(jnp.bfloat16),
            middle.astype(jnp.bfloat16),
            low.astype(jnp.bfloat16),
        )

    norm = jnp.zeros_like(points[0])
    for coord_index in range(points.shape[0]):
        norm = norm + points[coord_index] * points[coord_index]
    high, middle, low = split(points)
    norm_parts = jnp.stack(split(norm))
    ones = jnp.ones((3, points.shape[1]), jnp.bfloat16)
    pad = jnp.zeros((FEATURES - 6 * DIM - 6, points.shape[1]), jnp.bfloat16)
    twice = lambda part: part * jnp.asarray(-2.0, jnp.bfloat16)
    lhs = jnp.concatenate(
        [twice(high), twice(high), twice(middle), twice(middle), twice(high), twice(low), norm_parts, ones, pad]
    )
    rhs = jnp.concatenate([high, middle, high, middle, low, high, ones, norm_parts, pad])
    return lhs.T, rhs


def dense_kernel(rows_ref, leaf_ref, vec_ref, gate_ref, acc_ref, out_ref):
    del gate_ref, acc_ref
    squared = lax.dot_general(
        rows_ref[:, :FEATURES],
        leaf_ref[:, FEATURES : 2 * FEATURES],
        (((1,), (1,)), ((), ())),
        preferred_element_type=jnp.float32,
    )
    scaled = root_three * jnp.sqrt(jnp.maximum(squared, 0.0))
    kernel = ((1.0 + scaled) * jnp.exp(-scaled)).astype(jnp.bfloat16)
    out_ref[...] = jnp.dot(kernel, vec_ref[...], preferred_element_type=jnp.float32)


def dense_rows(acc, table, vec, gate, row_start, rows):
    leaf = row_start // LEAF
    first = row_start // BLOCK
    width = 2 * FEATURES
    return pl.pallas_call(
        dense_kernel,
        grid=(rows // BLOCK,),
        in_specs=[
            pl.BlockSpec((BLOCK, width), lambda i: (first + i, 0)),
            pl.BlockSpec((LEAF, width), lambda i: (leaf, 0)),
            pl.BlockSpec((LEAF, PANEL), lambda i: (leaf, 0)),
            pl.BlockSpec(memory_space=pl.ANY),
            pl.BlockSpec(memory_space=pl.ANY),
        ],
        out_specs=pl.BlockSpec((BLOCK, PANEL), lambda i: (first + i, 0)),
        out_shape=jax.ShapeDtypeStruct(acc.shape, jnp.float32),
        input_output_aliases={4: 0},
    )(table, table, vec, gate, acc)


def body(vectors, contexts, tree_order, live_counts, level_bases, coupling, length_scale):
    per_device = vectors.shape[0]
    leaf_count = live_counts.shape[0]
    local_levels = leaf_count.bit_length() - 1
    device_count = lax.axis_size("leaf")
    device_levels = device_count.bit_length() - 1
    slot_order = tree_order[0]
    onehot = (slot_order[:, None] == jnp.arange(per_device, dtype=jnp.int32)[None, :]).astype(
        jnp.bfloat16
    )
    lhs_features, rhs_features = gram_features(contexts / length_scale[:, None])
    table = lax.dot_general(
        onehot,
        jnp.concatenate([lhs_features, rhs_features.T, vectors], axis=1),
        (((1,), (0,)), ((), ())),
        preferred_element_type=jnp.float32,
    ).astype(jnp.bfloat16)
    ordered = table[:, 2 * FEATURES :]
    slot_limit = jnp.repeat(live_counts, LEAF)
    within = jnp.arange(per_device, dtype=jnp.int32) % LEAF
    live_rows = (within < slot_limit)[:, None]
    masked = jnp.where(live_rows, ordered, jnp.zeros_like(ordered))

    partials = jnp.einsum(
        "rp,lrk->lpk", masked, level_bases[local_levels:], preferred_element_type=jnp.float32
    )
    block_rows = min(512, LEAF)
    chunk_starts = list(range(0, per_device, block_rows))
    accumulated = jnp.zeros((per_device, PANEL), jnp.float32)
    stack = partials
    finished = []
    gate = jnp.zeros((8, RANK), jnp.float32)
    done = 0
    for bit_index in range(device_levels):
        received = swapped(stack, "leaf", bit_index)
        upto = (bit_index + 1) * len(chunk_starts) // device_levels
        for row_start in chunk_starts[done:upto]:
            accumulated = dense_rows(accumulated, table, masked, gate, row_start, block_rows)
        done = upto
        finished.append(received[0])
        stack = stack[1:] + received[1:]
        gate = received[0, :8]
    for row_start in chunk_starts[done:]:
        accumulated = dense_rows(accumulated, table, masked, gate, row_start, block_rows)
    sibling_totals = jnp.stack(finished)


    level_index = 0
    node_rows = LEAF * 2**level_index
    node_count = per_device // node_rows
    basis_nodes = level_bases[level_index].reshape(node_count, node_rows, RANK)
    vector_nodes = masked.reshape(node_count, node_rows, PANEL)
    node_sums = jnp.einsum(
        "nrp,nrk->npk", vector_nodes, basis_nodes, preferred_element_type=jnp.float32
    )
    node_coef = node_sums * (1.0 / math.sqrt(node_rows))
    sibling = node_coef.reshape(node_count // 2, 2, PANEL, RANK)[:, ::-1].reshape(
        node_count, PANEL, RANK
    )
    weights = (sibling * (coupling[level_index] / math.sqrt(RANK))).astype(jnp.bfloat16)
    accumulated = accumulated + jnp.einsum(
        "nrk,npk->nrp", basis_nodes, weights, preferred_element_type=jnp.float32
    ).reshape(per_device, PANEL)

    node_scale = jnp.array(
        [1.0 / math.sqrt(LEAF * 2 ** (local_levels + s)) for s in range(device_levels)],
        jnp.float32,
    )[:, None, None]
    node_coef = sibling_totals * node_scale
    weights = (node_coef * (coupling[local_levels:, None, :] / math.sqrt(RANK))).astype(
        jnp.bfloat16
    )
    accumulated = accumulated + jnp.einsum(
        "lrk,lpk->rp", level_bases[local_levels:], weights, preferred_element_type=jnp.float32
    )
    result = jnp.where(live_rows, accumulated, jnp.zeros_like(accumulated)).astype(jnp.bfloat16)
    inverse = (jnp.arange(per_device, dtype=jnp.int32)[:, None] == slot_order[None, :]).astype(
        jnp.bfloat16
    )
    return jnp.dot(inverse, result, preferred_element_type=jnp.float32).astype(jnp.bfloat16)


def solution(mesh):
    in_specs = (
        P("leaf", None),
        P(None, "leaf"),
        P("leaf", None),
        P("leaf"),
        P(None, "leaf", None),
        P(),
        P(),
    )
    out_specs = P("leaf", None)
    return jax.shard_map(body, mesh=mesh, in_specs=in_specs, out_specs=out_specs, check_vma=False)
```

```python
import math

import jax
import jax.numpy as jnp
from jax import lax
from jax.experimental import pallas as pl
from jax.sharding import PartitionSpec as P

LEAF = 2048
RANK = 128
PANEL = 64
DIM = 8


root_three = math.sqrt(3.0)
FEATURES = 64
BLOCK = 256


def swapped(x, axis, bit):
    return lax.ppermute(x, axis, [(i, i ^ 1 << bit) for i in range(lax.axis_size(axis))])


def gram_features(points):
    def split(value):
        high = lax.reduce_precision(value, exponent_bits=8, mantissa_bits=7)
        rest = value - high
        middle = lax.reduce_precision(rest, exponent_bits=8, mantissa_bits=7)
        low = rest - middle
        return (
            high.astype(jnp.bfloat16),
            middle.astype(jnp.bfloat16),
            low.astype(jnp.bfloat16),
        )

    norm = jnp.zeros_like(points[0])
    for coord_index in range(points.shape[0]):
        norm = norm + points[coord_index] * points[coord_index]
    high, middle, low = split(points)
    norm_parts = jnp.stack(split(norm))
    ones = jnp.ones((3, points.shape[1]), jnp.bfloat16)
    pad = jnp.zeros((FEATURES - 6 * DIM - 6, points.shape[1]), jnp.bfloat16)
    twice = lambda part: part * jnp.asarray(-2.0, jnp.bfloat16)
    lhs = jnp.concatenate(
        [twice(high), twice(high), twice(middle), twice(middle), twice(high), twice(low), norm_parts, ones, pad]
    )
    rhs = jnp.concatenate([high, middle, high, middle, low, high, ones, norm_parts, pad])
    return lhs.T, rhs


def dense_kernel(rows_ref, leaf_ref, vec_ref, gate_ref, *refs):
    out_ref = refs[-1]
    squared = lax.dot_general(
        rows_ref[:, :FEATURES],
        leaf_ref[:, FEATURES : 2 * FEATURES],
        (((1,), (1,)), ((), ())),
        preferred_element_type=jnp.float32,
    )
    scaled = root_three * jnp.sqrt(jnp.maximum(squared, 0.0))
    kernel = ((1.0 + scaled) * jnp.exp(-scaled)).astype(jnp.bfloat16)
    out_ref[...] = jnp.dot(kernel, vec_ref[...], preferred_element_type=jnp.float32)


def dense_rows(acc, table, vec, gate, row_start, rows):
    leaf = row_start // LEAF
    first = row_start // BLOCK
    width = 2 * FEATURES
    in_specs = [
        pl.BlockSpec((BLOCK, width), lambda i: (first + i, 0)),
        pl.BlockSpec((LEAF, width), lambda i: (leaf, 0)),
        pl.BlockSpec((LEAF, PANEL), lambda i: (leaf, 0)),
        pl.BlockSpec(memory_space=pl.ANY),
    ]
    operands = [table, table, vec, gate]
    aliases = {}
    if acc is not None:
        in_specs.append(pl.BlockSpec(memory_space=pl.ANY))
        operands.append(acc)
        aliases = {4: 0}
    return pl.pallas_call(
        dense_kernel,
        grid=(rows // BLOCK,),
        in_specs=in_specs,
        out_specs=pl.BlockSpec((BLOCK, PANEL), lambda i: (first + i, 0)),
        out_shape=jax.ShapeDtypeStruct((table.shape[0], PANEL), jnp.float32),
        input_output_aliases=aliases,
    )(*operands)


def body(vectors, contexts, tree_order, live_counts, level_bases, coupling, length_scale):
    per_device = vectors.shape[0]
    leaf_count = live_counts.shape[0]
    local_levels = leaf_count.bit_length() - 1
    device_count = lax.axis_size("leaf")
    device_levels = device_count.bit_length() - 1
    slot_order = tree_order[0]
    onehot = (slot_order[:, None] == jnp.arange(per_device, dtype=jnp.int32)[None, :]).astype(
        jnp.bfloat16
    )
    lhs_features, rhs_features = gram_features(contexts / length_scale[:, None])
    table = lax.dot_general(
        onehot,
        jnp.concatenate([lhs_features, rhs_features.T, vectors], axis=1),
        (((1,), (0,)), ((), ())),
        preferred_element_type=jnp.float32,
    ).astype(jnp.bfloat16)
    ordered = table[:, 2 * FEATURES :]
    slot_limit = jnp.repeat(live_counts, LEAF)
    within = jnp.arange(per_device, dtype=jnp.int32) % LEAF
    live_rows = (within < slot_limit)[:, None]
    masked = jnp.where(live_rows, ordered, jnp.zeros_like(ordered))

    partials = jnp.einsum(
        "rp,lrk->lpk", masked, level_bases[local_levels:], preferred_element_type=jnp.float32
    )
    block_rows = min(512, LEAF)
    chunk_starts = list(range(0, per_device, block_rows))
    accumulated = None
    stack = partials
    finished = []
    gate = jnp.zeros((8, RANK), jnp.float32)
    done = 0
    for bit_index in range(device_levels):
        received = swapped(stack, "leaf", bit_index)
        upto = (bit_index + 1) * len(chunk_starts) // device_levels
        for row_start in chunk_starts[done:upto]:
            accumulated = dense_rows(accumulated, table, masked, gate, row_start, block_rows)
        done = upto
        finished.append(received[0])
        stack = stack[1:] + received[1:]
        gate = received[0, :8]
    for row_start in chunk_starts[done:]:
        accumulated = dense_rows(accumulated, table, masked, gate, row_start, block_rows)
    sibling_totals = jnp.stack(finished)


    level_index = 0
    node_rows = LEAF * 2**level_index
    node_count = per_device // node_rows
    basis_nodes = level_bases[level_index].reshape(node_count, node_rows, RANK)
    vector_nodes = masked.reshape(node_count, node_rows, PANEL)
    node_sums = jnp.einsum(
        "nrp,nrk->npk", vector_nodes, basis_nodes, preferred_element_type=jnp.float32
    )
    node_coef = node_sums * (1.0 / math.sqrt(node_rows))
    sibling = node_coef.reshape(node_count // 2, 2, PANEL, RANK)[:, ::-1].reshape(
        node_count, PANEL, RANK
    )
    weights = (sibling * (coupling[level_index] / math.sqrt(RANK))).astype(jnp.bfloat16)
    accumulated = accumulated + jnp.einsum(
        "nrk,npk->nrp", basis_nodes, weights, preferred_element_type=jnp.float32
    ).reshape(per_device, PANEL)

    node_scale = jnp.array(
        [1.0 / math.sqrt(LEAF * 2 ** (local_levels + s)) for s in range(device_levels)],
        jnp.float32,
    )[:, None, None]
    node_coef = sibling_totals * node_scale
    weights = (node_coef * (coupling[local_levels:, None, :] / math.sqrt(RANK))).astype(
        jnp.bfloat16
    )
    accumulated = accumulated + jnp.einsum(
        "lrk,lpk->rp", level_bases[local_levels:], weights, preferred_element_type=jnp.float32
    )
    result = jnp.where(live_rows, accumulated, jnp.zeros_like(accumulated)).astype(jnp.bfloat16)
    inverse = (jnp.arange(per_device, dtype=jnp.int32)[:, None] == slot_order[None, :]).astype(
        jnp.bfloat16
    )
    return jnp.dot(inverse, result, preferred_element_type=jnp.float32).astype(jnp.bfloat16)


def solution(mesh):
    in_specs = (
        P("leaf", None),
        P(None, "leaf"),
        P("leaf", None),
        P("leaf"),
        P(None, "leaf", None),
        P(),
        P(),
    )
    out_specs = P("leaf", None)
    return jax.shard_map(body, mesh=mesh, in_specs=in_specs, out_specs=out_specs, check_vma=False)
```

```python
import math

import jax
import jax.numpy as jnp
from jax import lax
from jax.experimental import pallas as pl
from jax.sharding import PartitionSpec as P

LEAF = 2048
RANK = 128
PANEL = 64
DIM = 8


root_three = math.sqrt(3.0)
FEATURES = 64
BLOCK = 256


def swapped(x, axis, bit):
    return lax.ppermute(x, axis, [(i, i ^ 1 << bit) for i in range(lax.axis_size(axis))])


def gram_features(points):
    def split(value):
        high = lax.reduce_precision(value, exponent_bits=8, mantissa_bits=7)
        rest = value - high
        middle = lax.reduce_precision(rest, exponent_bits=8, mantissa_bits=7)
        low = rest - middle
        return (
            high.astype(jnp.bfloat16),
            middle.astype(jnp.bfloat16),
            low.astype(jnp.bfloat16),
        )

    norm = jnp.zeros_like(points[0])
    for coord_index in range(points.shape[0]):
        norm = norm + points[coord_index] * points[coord_index]
    high, middle, low = split(points)
    norm_parts = jnp.stack(split(norm))
    ones = jnp.ones((3, points.shape[1]), jnp.bfloat16)
    pad = jnp.zeros((FEATURES - 6 * DIM - 6, points.shape[1]), jnp.bfloat16)
    twice = lambda part: part * jnp.asarray(-2.0, jnp.bfloat16)
    lhs = jnp.concatenate(
        [twice(high), twice(high), twice(middle), twice(middle), twice(high), twice(low), norm_parts, ones, pad]
    )
    rhs = jnp.concatenate([high, middle, high, middle, low, high, ones, norm_parts, pad])
    return lhs.T, rhs


def dense_kernel(rows_ref, leaf_ref, vec_ref, gate_ref, *refs):
    out_ref = refs[-1]
    squared = lax.dot_general(
        rows_ref[:, :FEATURES],
        leaf_ref[:, FEATURES : 2 * FEATURES],
        (((1,), (1,)), ((), ())),
        preferred_element_type=jnp.float32,
    )
    scaled = root_three * jnp.sqrt(jnp.maximum(squared, 0.0))
    kernel = ((1.0 + scaled) * jnp.exp(-scaled)).astype(jnp.bfloat16)
    out_ref[...] = jnp.dot(kernel, vec_ref[...], preferred_element_type=jnp.float32)


def dense_rows(acc, table, vec, gate, row_start, rows):
    leaf = row_start // LEAF
    first = row_start // BLOCK
    width = 2 * FEATURES
    in_specs = [
        pl.BlockSpec((BLOCK, width), lambda i: (first + i, 0)),
        pl.BlockSpec((LEAF, width), lambda i: (leaf, 0)),
        pl.BlockSpec((LEAF, PANEL), lambda i: (leaf, 0)),
        pl.BlockSpec(memory_space=pl.ANY),
    ]
    operands = [table, table, vec, gate]
    aliases = {}
    if acc is not None:
        in_specs.append(pl.BlockSpec(memory_space=pl.ANY))
        operands.append(acc)
        aliases = {4: 0}
    return pl.pallas_call(
        dense_kernel,
        grid=(rows // BLOCK,),
        in_specs=in_specs,
        out_specs=pl.BlockSpec((BLOCK, PANEL), lambda i: (first + i, 0)),
        out_shape=jax.ShapeDtypeStruct((table.shape[0], PANEL), jnp.float32),
        input_output_aliases=aliases,
    )(*operands)


def body(vectors, contexts, tree_order, live_counts, level_bases, coupling, length_scale):
    per_device = vectors.shape[0]
    leaf_count = live_counts.shape[0]
    local_levels = leaf_count.bit_length() - 1
    device_count = lax.axis_size("leaf")
    device_levels = device_count.bit_length() - 1
    slot_order = tree_order[0]
    onehot = (slot_order[:, None] == jnp.arange(per_device, dtype=jnp.int32)[None, :]).astype(
        jnp.bfloat16
    )
    lhs_features, rhs_features = gram_features(contexts / length_scale[:, None])
    table = lax.dot_general(
        onehot,
        jnp.concatenate([lhs_features, rhs_features.T, vectors], axis=1),
        (((1,), (0,)), ((), ())),
        preferred_element_type=jnp.float32,
    ).astype(jnp.bfloat16)
    ordered = table[:, 2 * FEATURES :]
    slot_limit = jnp.repeat(live_counts, LEAF)
    within = jnp.arange(per_device, dtype=jnp.int32) % LEAF
    live_rows = (within < slot_limit)[:, None]
    masked = jnp.where(live_rows, ordered, jnp.zeros_like(ordered))

    partials = jnp.einsum(
        "rp,lrk->lpk", masked, level_bases[local_levels:], preferred_element_type=jnp.float32
    )
    block_rows = min(512, LEAF)
    chunk_starts = list(range(0, per_device, block_rows))
    accumulated = None
    stack = partials
    finished = []
    gate = jnp.zeros((8, RANK), jnp.float32)
    done = 0
    for bit_index in range(device_levels):
        received = swapped(stack, "leaf", bit_index)
        upto = (bit_index + 1) * len(chunk_starts) // device_levels
        for row_start in chunk_starts[done:upto]:
            accumulated = dense_rows(accumulated, table, masked, gate, row_start, block_rows)
        done = upto
        finished.append(received[0])
        stack = stack[1:] + received[1:]
        gate = received
    for row_start in chunk_starts[done:]:
        accumulated = dense_rows(accumulated, table, masked, gate, row_start, block_rows)
    sibling_totals = jnp.stack(finished)


    level_index = 0
    node_rows = LEAF * 2**level_index
    node_count = per_device // node_rows
    basis_nodes = level_bases[level_index].reshape(node_count, node_rows, RANK)
    vector_nodes = masked.reshape(node_count, node_rows, PANEL)
    node_sums = jnp.einsum(
        "nrp,nrk->npk", vector_nodes, basis_nodes, preferred_element_type=jnp.float32
    )
    node_coef = node_sums * (1.0 / math.sqrt(node_rows))
    sibling = node_coef.reshape(node_count // 2, 2, PANEL, RANK)[:, ::-1].reshape(
        node_count, PANEL, RANK
    )
    weights = (sibling * (coupling[level_index] / math.sqrt(RANK))).astype(jnp.bfloat16)
    accumulated = accumulated + jnp.einsum(
        "nrk,npk->nrp", basis_nodes, weights, preferred_element_type=jnp.float32
    ).reshape(per_device, PANEL)

    node_scale = jnp.array(
        [1.0 / math.sqrt(LEAF * 2 ** (local_levels + s)) for s in range(device_levels)],
        jnp.float32,
    )[:, None, None]
    node_coef = sibling_totals * node_scale
    weights = (node_coef * (coupling[local_levels:, None, :] / math.sqrt(RANK))).astype(
        jnp.bfloat16
    )
    accumulated = accumulated + jnp.einsum(
        "lrk,lpk->rp", level_bases[local_levels:], weights, preferred_element_type=jnp.float32
    )
    result = jnp.where(live_rows, accumulated, jnp.zeros_like(accumulated)).astype(jnp.bfloat16)
    inverse = (jnp.arange(per_device, dtype=jnp.int32)[:, None] == slot_order[None, :]).astype(
        jnp.bfloat16
    )
    return jnp.dot(inverse, result, preferred_element_type=jnp.float32).astype(jnp.bfloat16)


def solution(mesh):
    in_specs = (
        P("leaf", None),
        P(None, "leaf"),
        P("leaf", None),
        P("leaf"),
        P(None, "leaf", None),
        P(),
        P(),
    )
    out_specs = P("leaf", None)
    return jax.shard_map(body, mesh=mesh, in_specs=in_specs, out_specs=out_specs, check_vma=False)
```

```python
import math

import jax
import jax.numpy as jnp
from jax import lax
from jax.experimental import pallas as pl
from jax.sharding import PartitionSpec as P

LEAF = 2048
RANK = 128
PANEL = 64
DIM = 8


root_three = math.sqrt(3.0)
FEATURES = 64
BLOCK = 256


def swapped(x, axis, bit):
    return lax.ppermute(x, axis, [(i, i ^ 1 << bit) for i in range(lax.axis_size(axis))])


def gram_features(points):
    def split(value):
        high = lax.reduce_precision(value, exponent_bits=8, mantissa_bits=7)
        rest = value - high
        middle = lax.reduce_precision(rest, exponent_bits=8, mantissa_bits=7)
        low = rest - middle
        return (
            high.astype(jnp.bfloat16),
            middle.astype(jnp.bfloat16),
            low.astype(jnp.bfloat16),
        )

    norm = jnp.zeros_like(points[0])
    for coord_index in range(points.shape[0]):
        norm = norm + points[coord_index] * points[coord_index]
    high, middle, low = split(points)
    norm_parts = jnp.stack(split(norm))
    ones = jnp.ones((3, points.shape[1]), jnp.bfloat16)
    pad = jnp.zeros((FEATURES - 6 * DIM - 6, points.shape[1]), jnp.bfloat16)
    twice = lambda part: part * jnp.asarray(-2.0, jnp.bfloat16)
    lhs = jnp.concatenate(
        [twice(high), twice(high), twice(middle), twice(middle), twice(high), twice(low), norm_parts, ones, pad]
    )
    rhs = jnp.concatenate([high, middle, high, middle, low, high, ones, norm_parts, pad])
    return lhs.T, rhs


def dense_kernel(rows_ref, leaf_ref, vec_ref, gate_ref, *refs):
    out_ref = refs[-1]
    squared = lax.dot_general(
        rows_ref[:, :FEATURES],
        leaf_ref[:, FEATURES : 2 * FEATURES],
        (((1,), (1,)), ((), ())),
        preferred_element_type=jnp.float32,
    )
    scaled = root_three * jnp.sqrt(jnp.maximum(squared, 0.0))
    kernel = ((1.0 + scaled) * jnp.exp(-scaled)).astype(jnp.bfloat16)
    out_ref[...] = jnp.dot(kernel, vec_ref[...], preferred_element_type=jnp.float32)


def dense_rows(acc, table, vec, gate, row_start, rows):
    leaf = row_start // LEAF
    first = row_start // BLOCK
    width = 2 * FEATURES
    in_specs = [
        pl.BlockSpec((BLOCK, width), lambda i: (first + i, 0)),
        pl.BlockSpec((LEAF, width), lambda i: (leaf, 0)),
        pl.BlockSpec((LEAF, PANEL), lambda i: (leaf, 0)),
        pl.BlockSpec(memory_space=pl.ANY),
    ]
    operands = [table, table, vec, gate]
    aliases = {}
    if acc is not None:
        in_specs.append(pl.BlockSpec(memory_space=pl.ANY))
        operands.append(acc)
        aliases = {4: 0}
    return pl.pallas_call(
        dense_kernel,
        grid=(rows // BLOCK,),
        in_specs=in_specs,
        out_specs=pl.BlockSpec((BLOCK, PANEL), lambda i: (first + i, 0)),
        out_shape=jax.ShapeDtypeStruct((table.shape[0], PANEL), jnp.float32),
        input_output_aliases=aliases,
    )(*operands)


def body(vectors, contexts, tree_order, live_counts, level_bases, coupling, length_scale):
    per_device = vectors.shape[0]
    leaf_count = live_counts.shape[0]
    local_levels = leaf_count.bit_length() - 1
    device_count = lax.axis_size("leaf")
    device_levels = device_count.bit_length() - 1
    slot_order = tree_order[0]
    slot_limit = jnp.repeat(live_counts, LEAF)
    within = jnp.arange(per_device, dtype=jnp.int32) % LEAF
    live_rows = (within < slot_limit)[:, None]
    onehot = (
        (slot_order[:, None] == jnp.arange(per_device, dtype=jnp.int32)[None, :]) & live_rows
    ).astype(jnp.bfloat16)
    lhs_features, rhs_features = gram_features(contexts / length_scale[:, None])
    table = lax.dot_general(
        onehot,
        jnp.concatenate([lhs_features, rhs_features.T, vectors], axis=1),
        (((1,), (0,)), ((), ())),
        preferred_element_type=jnp.float32,
    ).astype(jnp.bfloat16)
    masked = table[:, 2 * FEATURES :]

    partials = jnp.einsum(
        "rp,lrk->lpk", masked, level_bases[local_levels:], preferred_element_type=jnp.float32
    )
    block_rows = min(512, LEAF)
    chunk_starts = list(range(0, per_device, block_rows))
    accumulated = None
    stack = partials
    finished = []
    gate = jnp.zeros((8, RANK), jnp.float32)
    done = 0
    for bit_index in range(device_levels):
        received = swapped(stack, "leaf", bit_index)
        upto = (bit_index + 1) * len(chunk_starts) // device_levels
        for row_start in chunk_starts[done:upto]:
            accumulated = dense_rows(accumulated, table, masked, gate, row_start, block_rows)
        done = upto
        finished.append(received[0])
        stack = stack[1:] + received[1:]
        gate = received[0, :8]
    for row_start in chunk_starts[done:]:
        accumulated = dense_rows(accumulated, table, masked, gate, row_start, block_rows)
    sibling_totals = jnp.stack(finished)


    level_index = 0
    node_rows = LEAF * 2**level_index
    node_count = per_device // node_rows
    basis_nodes = level_bases[level_index].reshape(node_count, node_rows, RANK)
    vector_nodes = masked.reshape(node_count, node_rows, PANEL)
    node_sums = jnp.einsum(
        "nrp,nrk->npk", vector_nodes, basis_nodes, preferred_element_type=jnp.float32
    )
    node_coef = node_sums * (1.0 / math.sqrt(node_rows))
    sibling = node_coef.reshape(node_count // 2, 2, PANEL, RANK)[:, ::-1].reshape(
        node_count, PANEL, RANK
    )
    weights = (sibling * (coupling[level_index] / math.sqrt(RANK))).astype(jnp.bfloat16)
    accumulated = accumulated + jnp.einsum(
        "nrk,npk->nrp", basis_nodes, weights, preferred_element_type=jnp.float32
    ).reshape(per_device, PANEL)

    node_scale = jnp.array(
        [1.0 / math.sqrt(LEAF * 2 ** (local_levels + s)) for s in range(device_levels)],
        jnp.float32,
    )[:, None, None]
    node_coef = sibling_totals * node_scale
    weights = (node_coef * (coupling[local_levels:, None, :] / math.sqrt(RANK))).astype(
        jnp.bfloat16
    )
    accumulated = accumulated + jnp.einsum(
        "lrk,lpk->rp", level_bases[local_levels:], weights, preferred_element_type=jnp.float32
    )
    result = jnp.where(live_rows, accumulated, jnp.zeros_like(accumulated)).astype(jnp.bfloat16)
    inverse = (jnp.arange(per_device, dtype=jnp.int32)[:, None] == slot_order[None, :]).astype(
        jnp.bfloat16
    )
    return jnp.dot(inverse, result, preferred_element_type=jnp.float32).astype(jnp.bfloat16)


def solution(mesh):
    in_specs = (
        P("leaf", None),
        P(None, "leaf"),
        P("leaf", None),
        P("leaf"),
        P(None, "leaf", None),
        P(),
        P(),
    )
    out_specs = P("leaf", None)
    return jax.shard_map(body, mesh=mesh, in_specs=in_specs, out_specs=out_specs, check_vma=False)
```
